256 devices in a mesh: dp: 4 (over x), seq: 64 (over y, z, core).
Axes of the slice: x: 4, y: 4, z: 8, core: 2. Of those that a mesh axis runs over, the one named last changes fastest.
Arguments:
- queries: bfloat16 [4, 8192, 8192], P('dp', 'seq'), may hold values from -75 to 75
- cotangent: bfloat16 [4, 8192, 8192], P('dp', 'seq'), may hold values from -6 to 6
- states: bfloat16 [64, 64, 16384], P('seq'), may hold values from -5 to 5
- neighbours: int32 [4, 128, 2], P('dp'), may hold values from 0 to 62, as said below
Outputs:
- attended: bfloat16 [4, 8192, 8192], P('dp', 'seq')
- query_grad: bfloat16 [4, 8192, 8192], P('dp', 'seq')
- state_grad: bfloat16 [64, 64, 16384], P('seq')
The draws below stay inside these ranges and needn't reach their ends.
Inputs may be any that keep to these rules, and one draw needn't show every extreme that they name: `neighbours`: low ids are retrieved more often than high ones.
All inputs are finite; a program needn't handle non-finite values.
Results may differ from the reference program's by a relative error of at most 0.009.
Values may be sent and summed in bfloat16 or wider, within the bound.
No kernel may reach another device: no remote copies, remote signals or barrier semaphores. Data moves between devices by JAX's collectives and lax.ppermute only.
A program may use at most 128 MiB of HBM per device.

```python
import math
import jax
import jax.numpy as jnp
from jax import lax

HD = 128
SPAN = 64
HEADS = 64
D = 8192
LEN = 8192
SPANS = 128
UNITS = 64
SEQS = 4


def neighbour_table(key):
    base = jax.random.fold_in(key, 101)
    parts = jax.random.split(base, 4)
    shape = (SEQS, SPANS * 2)
    first = jax.random.randint(parts[0], shape, 0, UNITS - 1)
    second = jax.random.randint(parts[1], shape, 0, UNITS - 1)
    table = jnp.minimum(first, second)
    spots = jnp.arange(SPANS * 2, dtype=jnp.int32)[None, :]
    high_at = jax.random.randint(parts[2], (SEQS, 1), 0, SPANS * 2)
    low_at = jax.random.randint(parts[3], (SEQS, 1), 0, SPANS * 2)
    table = jnp.where(spots == low_at, 0, table)
    table = jnp.where(spots == high_at, UNITS - 2, table)
    return table.reshape(SEQS, SPANS, 2).astype(jnp.int32)


def draw_neighbours(key, part):
    return neighbour_table(key)


def draw_states(key, part):
    both = jnp.clip(jax.random.normal(jax.random.fold_in(key, 404), (UNITS, SPAN, 2, HEADS, HD), jnp.float32), -5.0, 5.0)
    return both.reshape(UNITS, SPAN, 2 * HEADS * HD).astype(jnp.bfloat16)


def draw_queries(key, part):
    shape = (SEQS, LEN, HEADS, HD)
    full = jnp.clip(jax.random.normal(jax.random.fold_in(key, 606), shape, jnp.float32), -5.0, 5.0)
    return full.reshape(SEQS, LEN, HEADS * HD).astype(jnp.bfloat16)


def steps_of(stream_key, extent, pieces, least, top_value):
    def one(position, blocks):
        steps = jax.random.uniform(jax.random.fold_in(jax.random.fold_in(stream_key, 6), position), (blocks,), jnp.float32, least / len(pieces), top_value / len(pieces))
        return jnp.repeat(jnp.exp(steps), extent[position] // blocks).reshape((-1,) + (1,) * (len(extent) - position - 1))

    gain = one(*pieces[0])
    for cut in pieces[1:]:
        gain = gain * one(*cut)
    return gain


def noise(key, shape, spread, most, shards=(), kind=jnp.bfloat16):
    drawn = spread * jax.random.normal(key, shape, jnp.float32)
    if shards:
        drawn = drawn * steps_of(key, shape, shards, -0.22, 0.18)
    return jnp.clip(drawn, -most, most).astype(kind)


def setup_inputs(seed: int = 0) -> dict:
    seeds = jax.random.split(jax.random.key(seed), 5)
    return {
        "queries": draw_queries(jax.random.fold_in(seeds[4], 71), 0),
        "cotangent": noise(seeds[1], (SEQS, LEN, D), 1.0, 6.0, ((0, 4), (1, 64))),
        "states": draw_states(jax.random.fold_in(seeds[4], 71), 0),
        "neighbours": draw_neighbours(jax.random.fold_in(seeds[4], 71), 0),
    }


def attend_heads(queries, cotangent, states, neighbours):
    length = queries.shape[0]
    heads = queries.shape[1]
    size_head = queries.shape[2]
    units_all = states.shape[0]
    margin = SPAN - 1
    spans_all = length // SPAN
    per_block = math.gcd(512 // SPAN, spans_all)
    blocks = spans_all // per_block
    tail = jnp.zeros((margin, heads, size_head), queries.dtype)
    query_win = jnp.concatenate([queries[margin:], tail], axis=0).reshape(blocks, per_block, SPAN, heads, size_head)
    grad_win = jnp.concatenate([cotangent[margin:], tail], axis=0).reshape(blocks, per_block, SPAN, heads, size_head)
    first = neighbours[:, 0].astype(jnp.int32)
    second = neighbours[:, 1].astype(jnp.int32)
    picked = jnp.stack([first, first + 1, second, second + 1], axis=1).reshape(blocks, per_block, 4)
    scale = 1.0 / math.sqrt(size_head)

    def step(total, items):
        query_blk, grad_blk, pick_blk = items
        gathered = states[pick_blk].reshape(per_block, 4 * SPAN, 2, heads, size_head)
        keys = gathered[:, :, 0].astype(jnp.float32)
        values = gathered[:, :, 1].astype(jnp.float32)
        query_f = query_blk.astype(jnp.float32)
        grad_f = grad_blk.astype(jnp.float32)
        scores = jnp.einsum('cihd,cjhd->chij', query_f, keys) * scale
        top = lax.optimization_barrier(jnp.max(scores, axis=-1, keepdims=True))
        expo = jnp.exp(scores - top)
        probs = expo / lax.optimization_barrier(jnp.sum(expo, axis=-1, keepdims=True))
        probs_low = lax.optimization_barrier(probs.astype(jnp.bfloat16)).astype(jnp.float32)
        attended = jnp.einsum('chij,cjhd->cihd', probs_low, values)
        grad_probs = jnp.einsum('cihd,cjhd->chij', grad_f, values)
        delta = lax.optimization_barrier(jnp.sum(probs * grad_probs, axis=-1, keepdims=True))
        grad_scores = lax.optimization_barrier((probs * (grad_probs - delta) * scale).astype(jnp.bfloat16)).astype(jnp.float32)
        grad_query = jnp.einsum('chij,cjhd->cihd', grad_scores, keys)
        grad_keys = jnp.einsum('chij,cihd->cjhd', grad_scores, query_f)
        grad_values = jnp.einsum('chij,cihd->cjhd', probs_low, grad_f)
        pair = jnp.stack([grad_keys, grad_values], axis=2).reshape(per_block * 4, SPAN, 2, heads, size_head)
        total = total + jax.ops.segment_sum(pair, pick_blk.reshape(-1), num_segments=units_all)
        return (total, (attended.astype(jnp.bfloat16), grad_query.astype(jnp.bfloat16)))
    init = jnp.zeros((units_all, SPAN, 2, heads, size_head), jnp.float32)
    total, outputs = lax.scan(step, init, (query_win, grad_win, picked))
    lead = jnp.zeros((margin, heads, size_head), jnp.bfloat16)
    attended = jnp.concatenate([lead, outputs[0].reshape(length, heads, size_head)[:length - margin]], axis=0)
    grad_query = jnp.concatenate([lead, outputs[1].reshape(length, heads, size_head)[:length - margin]], axis=0)
    return (attended, grad_query, total)

def reference(queries, cotangent, states, neighbours):
    kv_all = states.reshape(UNITS, SPAN, 2, HEADS, HD)
    kv_heads = jnp.transpose(kv_all, (3, 0, 1, 2, 4))[:, :, :, :, None, :]
    grad_total = jnp.zeros((HEADS, UNITS, SPAN, 2, 1, HD), jnp.float32)
    attended_list = []
    grad_list = []
    for seq_index in range(SEQS):
        q_heads = jnp.transpose(queries[seq_index].reshape(LEN, HEADS, HD), (1, 0, 2))[:, :, None, :]
        g_heads = jnp.transpose(cotangent[seq_index].reshape(LEN, HEADS, HD), (1, 0, 2))[:, :, None, :]
        table = neighbours[seq_index]

        def one_head(items):
            return attend_heads(items[0], items[1], items[2], table)
        attended, grad_query, unit_grads = lax.map(one_head, (q_heads, g_heads, kv_heads))
        attended_list.append(jnp.transpose(attended[:, :, 0, :], (1, 0, 2)).reshape(LEN, HEADS * HD))
        grad_list.append(jnp.transpose(grad_query[:, :, 0, :], (1, 0, 2)).reshape(LEN, HEADS * HD))
        grad_total = grad_total + lax.optimization_barrier(unit_grads.astype(jnp.bfloat16)).astype(jnp.float32)
    state_grad = jnp.transpose(grad_total[:, :, :, :, 0, :], (1, 2, 3, 0, 4)).reshape(UNITS, SPAN, 2 * HEADS * HD)
    return (jnp.stack(attended_list, axis=0), jnp.stack(grad_list, axis=0), state_grad.astype(jnp.bfloat16))
```

```python
import functools
import math

import jax
import jax.numpy as jnp
from jax import lax
from jax.experimental import pallas as pl
from jax.experimental.pallas import tpu as pltpu
from jax.sharding import PartitionSpec as P

SPAN = 64
HD = 128
NT = (((1,), (1,)), ((), ()))
TN = (((0,), (0,)), ((), ()))


def _part(q, g, kv_ref, acc_ref, nb_ref, span, valid, scale):
    u0 = nb_ref[2 * span]
    u1 = nb_ref[2 * span + 1]
    units = (u0, u0 + 1, u1, u1 + 1)
    kv = jnp.concatenate([kv_ref[u] for u in units], axis=0)
    k = kv[:, :HD]
    v = kv[:, HD:]
    s = lax.dot_general(q, k, NT, preferred_element_type=jnp.float32) * scale
    top = jnp.max(s, axis=1, keepdims=True)
    e = jnp.exp(s - top)
    p = e / jnp.sum(e, axis=1, keepdims=True)
    p = jnp.where(valid, p, 0.0)
    p_low = p.astype(jnp.bfloat16)
    att = jnp.dot(p_low, v, preferred_element_type=jnp.float32)
    gp = lax.dot_general(g, v, NT, preferred_element_type=jnp.float32)
    delta = jnp.sum(p * gp, axis=1, keepdims=True)
    gs = (p * (gp - delta) * scale).astype(jnp.bfloat16)
    gq = jnp.dot(gs, k, preferred_element_type=jnp.float32)
    dk = lax.dot_general(gs, q, TN, preferred_element_type=jnp.float32)
    dv = lax.dot_general(p_low, g, TN, preferred_element_type=jnp.float32)
    dkv = jnp.concatenate([dk, dv], axis=1)
    for t, u in enumerate(units):
        acc_ref[u] += dkv[SPAN * t:SPAN * (t + 1)]
    return att, gq


def _kernel(chunk, first, nb_ref, q_ref, g_ref, kv_ref, *rest):
    if first:
        att_ref, gq_ref, acc_ref = rest
    else:
        acc_in_ref, att_ref, gq_ref, acc_ref = rest
    j = pl.program_id(0)

    @pl.when(j == 0)
    def _():
        if first:
            acc_ref[...] = jnp.zeros(acc_ref.shape, acc_ref.dtype)
        else:
            acc_ref[...] = acc_in_ref[...]

    scale = 1.0 / math.sqrt(HD)
    rows = q_ref.shape[0]
    tail = 16
    b = 2 * j + chunk
    q = q_ref[...]
    g = g_ref[...]
    row = lax.broadcasted_iota(jnp.int32, (rows, 1), 0)
    valid1 = (row < rows - 1) & (b >= 1)
    att1, gq1 = _part(q, g, kv_ref, acc_ref, nb_ref, jnp.maximum(b - 1, 0), valid1, scale)
    row2 = lax.broadcasted_iota(jnp.int32, (tail, 1), 0)
    valid2 = row2 == tail - 1
    att2, gq2 = _part(q[rows - tail:], g[rows - tail:], kv_ref, acc_ref, nb_ref, b, valid2, scale)
    att = jnp.concatenate([att1[:rows - tail], att1[rows - tail:] + att2], axis=0)
    gq = jnp.concatenate([gq1[:rows - tail], gq1[rows - tail:] + gq2], axis=0)
    att_ref[...] = att.astype(att_ref.dtype)
    gq_ref[...] = gq.astype(gq_ref.dtype)


def attend_chunk(chunk, nb, q, g, kv, acc):
    pieces, rows, _ = q.shape
    units = kv.shape[0]
    first = acc is None
    tok = pl.BlockSpec((None, rows, HD), lambda j, nb: (j, 0, 0))
    whole_kv = pl.BlockSpec(kv.shape, lambda j, nb: (0, 0, 0))
    acc_shape = (units, SPAN, 2 * HD)
    whole_acc = pl.BlockSpec(acc_shape, lambda j, nb: (0, 0, 0))
    in_specs = [tok, tok, whole_kv] + ([] if first else [whole_acc])
    flops = pieces * (rows + 16) * 4 * SPAN * HD * 2 * 6
    bytes_accessed = 4 * q.size * 2 + kv.size * 2 + math.prod(acc_shape) * 4 * (1 if first else 2)
    call = pl.pallas_call(
        functools.partial(_kernel, chunk, first),
        grid_spec=pltpu.PrefetchScalarGridSpec(
            num_scalar_prefetch=1,
            grid=(pieces,),
            in_specs=in_specs,
            out_specs=[tok, tok, whole_acc],
        ),
        out_shape=[
            jax.ShapeDtypeStruct(q.shape, jnp.bfloat16),
            jax.ShapeDtypeStruct(q.shape, jnp.bfloat16),
            jax.ShapeDtypeStruct(acc_shape, jnp.float32),
        ],
        input_output_aliases={} if first else {4: 2},
        compiler_params=pltpu.CompilerParams(
            dimension_semantics=("arbitrary",), vmem_limit_bytes=56 * 1024 * 1024
        ),
        cost_estimate=pl.CostEstimate(
            flops=flops, transcendentals=pieces * (rows + 16) * 4 * SPAN, bytes_accessed=bytes_accessed
        ),
        name=f"attend_chunk{chunk}",
    )
    args = (nb, q, g, kv) if first else (nb, q, g, kv, acc)
    return call(*args)


def local(queries, cotangent, states, neighbours):
    parts = lax.axis_size("seq")
    groups = lax.axis_size("dp")
    tok_dev = queries.shape[1]
    width = queries.shape[2]
    heads = width // HD
    quarter = SPAN // groups
    member = lax.axis_index("dp")

    st = states.reshape(SPAN, 2, heads, HD)
    st = lax.dynamic_slice_in_dim(st, member * quarter, quarter, axis=0)[None]
    moved = lax.all_to_all(st, "seq", split_axis=3, concat_axis=0, tiled=True)
    kv = lax.all_gather(moved, "dp", axis=1, tiled=True).reshape(parts, SPAN, 2 * HD)
    nb = neighbours.reshape(-1)

    q = queries.reshape(tok_dev, heads, HD)
    g = cotangent.reshape(tok_dev, heads, HD)
    half = tok_dev // 2
    acc = None
    att_rows, gq_rows = [], []
    for chunk in range(2):
        sl = slice(chunk * half, (chunk + 1) * half)
        qk = lax.all_to_all(q[sl], "seq", split_axis=1, concat_axis=0, tiled=True)
        gk = lax.all_to_all(g[sl], "seq", split_axis=1, concat_axis=0, tiled=True)
        qk = qk.reshape(parts, half, HD)
        gk = gk.reshape(parts, half, HD)
        att, gq, acc = attend_chunk(chunk, nb, qk, gk, kv, acc)
        att = lax.all_to_all(att.reshape(parts, half, 1, HD), "seq", split_axis=0, concat_axis=2, tiled=True)
        gq = lax.all_to_all(gq.reshape(parts, half, 1, HD), "seq", split_axis=0, concat_axis=2, tiled=True)
        att_rows.append(att.reshape(half, width))
        gq_rows.append(gq.reshape(half, width))
    attended = jnp.concatenate(att_rows, axis=0).reshape(1, tok_dev, width)
    query_grad = jnp.concatenate(gq_rows, axis=0).reshape(1, tok_dev, width)

    red = lax.psum_scatter(acc, "dp", scatter_dimension=1, tiled=True).astype(jnp.bfloat16)
    home = lax.all_to_all(red, "seq", split_axis=0, concat_axis=0, tiled=True)
    home = home.reshape(heads, quarter, 2, HD).transpose(1, 2, 0, 3).reshape(quarter, 2 * width)
    state_grad = lax.all_gather(home, "dp", axis=0, tiled=True).reshape(1, SPAN, 2 * width)
    return (attended, query_grad, state_grad)


def solution(mesh):
    placed = (P("dp", "seq", None), P("dp", "seq", None), P("seq", None, None), P("dp", None, None))
    return jax.shard_map(
        local,
        mesh=mesh,
        in_specs=placed,
        out_specs=(P("dp", "seq", None), P("dp", "seq", None), P("seq", None, None)),
        check_vma=False,
    )
```

```python
import functools
import math

import jax
import jax.numpy as jnp
from jax import lax
from jax.experimental import pallas as pl
from jax.experimental.pallas import tpu as pltpu
from jax.sharding import PartitionSpec as P

SPAN = 64
HD = 128
NT = (((1,), (1,)), ((), ()))
TN = (((0,), (0,)), ((), ()))


def _span(qg, kv_ref, acc_ref, nb_ref, span, valid, scale):
    q = qg[:, :HD]
    g = qg[:, HD:]
    u0 = nb_ref[2 * span]
    u1 = nb_ref[2 * span + 1]
    units = (u0, u0 + 1, u1, u1 + 1)
    kv = jnp.concatenate([kv_ref[u] for u in units], axis=0)
    k = kv[:, :HD]
    v = kv[:, HD:]
    s = lax.dot_general(q, k, NT, preferred_element_type=jnp.float32) * scale
    top = jnp.max(s, axis=1, keepdims=True)
    e = jnp.exp(s - top)
    p = e / jnp.sum(e, axis=1, keepdims=True)
    if valid is not None:
        p = jnp.where(valid, p, 0.0)
    p_low = p.astype(jnp.bfloat16)
    att = jnp.dot(p_low, v, preferred_element_type=jnp.float32)
    gp = lax.dot_general(g, v, NT, preferred_element_type=jnp.float32)
    delta = jnp.sum(p * gp, axis=1, keepdims=True)
    gs = (p * (gp - delta) * scale).astype(jnp.bfloat16)
    gq = jnp.dot(gs, k, preferred_element_type=jnp.float32)
    dk = lax.dot_general(gs, q, TN, preferred_element_type=jnp.float32)
    dv = lax.dot_general(p_low, g, TN, preferred_element_type=jnp.float32)
    dkv = jnp.concatenate([dk, dv], axis=1)
    for t, u in enumerate(units):
        acc_ref[u] += dkv[SPAN * t:SPAN * (t + 1)]
    return jnp.concatenate([att, gq], axis=1)


def _kernel(chunk, first, per, nb_ref, qg_ref, kv_ref, *rest):
    if first:
        out_ref, acc_ref = rest
    else:
        acc_in_ref, out_ref, acc_ref = rest
    j = pl.program_id(0)

    @pl.when(j == 0)
    def _():
        if first:
            acc_ref[...] = jnp.zeros(acc_ref.shape, acc_ref.dtype)
        else:
            acc_ref[...] = acc_in_ref[...]

    scale = 1.0 / math.sqrt(HD)
    pieces, rows, _ = qg_ref.shape
    row = lax.broadcasted_iota(jnp.int32, (rows, 1), 0)
    for t in range(per):
        piece = per * j + t
        if chunk == 0:
            out = _span(qg_ref[piece], kv_ref, acc_ref, nb_ref, 2 * piece, None, scale)
            out_ref[piece] = out.astype(out_ref.dtype)
        else:
            prev = (piece + pieces - 1) % pieces
            head = row == 0
            tile = jnp.where(
                head, qg_ref[prev].astype(jnp.float32), qg_ref[piece].astype(jnp.float32)
            ).astype(jnp.bfloat16)
            span = (2 * piece + 2 * pieces - 1) % (2 * pieces)
            valid = head | (piece >= 1)
            out = _span(tile, kv_ref, acc_ref, nb_ref, span, valid, scale)
            mine = out_ref[piece].astype(jnp.float32)
            out_ref[piece] = jnp.where(head, mine, out).astype(out_ref.dtype)
            before = out_ref[prev].astype(jnp.float32)
            out_ref[prev] = jnp.where(head, out, before).astype(out_ref.dtype)


def attend_chunk(chunk, nb, qg, kv, acc, per=2):
    pieces, rows, lanes = qg.shape
    units = kv.shape[0]
    first = acc is None
    whole_qg = pl.BlockSpec(qg.shape, lambda j, nb: (0, 0, 0))
    whole_kv = pl.BlockSpec(kv.shape, lambda j, nb: (0, 0, 0))
    acc_shape = (units, SPAN, 2 * HD)
    whole_acc = pl.BlockSpec(acc_shape, lambda j, nb: (0, 0, 0))
    in_specs = [whole_qg, whole_kv] + ([] if first else [whole_acc])
    flops = pieces * rows * 4 * SPAN * HD * 2 * 6
    bytes_accessed = 2 * qg.size * 2 + kv.size * 2 + math.prod(acc_shape) * 4 * (1 if first else 2)
    call = pl.pallas_call(
        functools.partial(_kernel, chunk, first, per),
        grid_spec=pltpu.PrefetchScalarGridSpec(
            num_scalar_prefetch=1,
            grid=(pieces // per,),
            in_specs=in_specs,
            out_specs=[whole_qg, whole_acc],
        ),
        out_shape=[
            jax.ShapeDtypeStruct(qg.shape, jnp.bfloat16),
            jax.ShapeDtypeStruct(acc_shape, jnp.float32),
        ],
        input_output_aliases={} if first else {3: 1},
        compiler_params=pltpu.CompilerParams(
            dimension_semantics=("arbitrary",), vmem_limit_bytes=56 * 1024 * 1024
        ),
        cost_estimate=pl.CostEstimate(
            flops=flops, transcendentals=pieces * rows * 4 * SPAN, bytes_accessed=bytes_accessed
        ),
        name=f"attend_chunk{chunk}",
    )
    args = (nb, qg, kv) if first else (nb, qg, kv, acc)
    return call(*args)


def local(queries, cotangent, states, neighbours):
    parts = lax.axis_size("seq")
    groups = lax.axis_size("dp")
    tok_dev = queries.shape[1]
    width = queries.shape[2]
    heads = width // HD
    quarter = SPAN // groups
    member = lax.axis_index("dp")

    st = states.reshape(SPAN, 2, heads, HD)
    st = lax.dynamic_slice_in_dim(st, member * quarter, quarter, axis=0)[None]
    moved = lax.all_to_all(st, "seq", split_axis=3, concat_axis=0, tiled=True)
    kv = lax.all_gather(moved, "dp", axis=1, tiled=True).reshape(parts, SPAN, 2 * HD)
    nb = neighbours.reshape(-1)

    both = jnp.stack(
        [queries.reshape(tok_dev, heads, HD), cotangent.reshape(tok_dev, heads, HD)], axis=2
    )
    lead = SPAN - 1
    chunks = (
        both[lead:lead + SPAN],
        jnp.concatenate([both[tok_dev - 1:], both[:lead]], axis=0),
    )
    acc = None
    outs = []
    for chunk, part in enumerate(chunks):
        qg = lax.all_to_all(part, "seq", split_axis=1, concat_axis=0, tiled=True)
        out, acc = attend_chunk(chunk, nb, qg.reshape(parts, SPAN, 2 * HD), kv, acc)
        out = lax.all_to_all(
            out.reshape(parts, SPAN, 1, 2, HD), "seq", split_axis=0, concat_axis=2, tiled=True
        )
        outs.append(out.reshape(SPAN, heads, 2, HD))
    rows = jnp.concatenate([outs[1][1:], outs[0], outs[1][:1]], axis=0)
    attended = rows[:, :, 0].reshape(1, tok_dev, width)
    query_grad = rows[:, :, 1].reshape(1, tok_dev, width)

    red = lax.psum_scatter(acc, "dp", scatter_dimension=1, tiled=True).astype(jnp.bfloat16)
    home = lax.all_to_all(red, "seq", split_axis=0, concat_axis=0, tiled=True)
    home = home.reshape(heads, quarter, 2, HD).transpose(1, 2, 0, 3).reshape(quarter, 2 * width)
    state_grad = lax.all_gather(home, "dp", axis=0, tiled=True).reshape(1, SPAN, 2 * width)
    return (attended, query_grad, state_grad)


def solution(mesh):
    placed = (P("dp", "seq", None), P("dp", "seq", None), P("seq", None, None), P("dp", None, None))
    return jax.shard_map(
        local,
        mesh=mesh,
        in_specs=placed,
        out_specs=(P("dp", "seq", None), P("dp", "seq", None), P("seq", None, None)),
        check_vma=False,
    )
```

```python
import functools
import math

import jax
import jax.numpy as jnp
from jax import lax
from jax.experimental import pallas as pl
from jax.experimental.pallas import tpu as pltpu
from jax.sharding import PartitionSpec as P

SPAN = 64
HD = 128
NT = (((1,), (1,)), ((), ()))
TN = (((0,), (0,)), ((), ()))


def _span(qg, kv_ref, acc_ref, nb_ref, span, valid, scale):
    q = qg[:, :HD]
    g = qg[:, HD:]
    u0 = nb_ref[2 * span]
    u1 = nb_ref[2 * span + 1]
    units = (u0, u0 + 1, u1, u1 + 1)
    kv = jnp.concatenate([kv_ref[u] for u in units], axis=0)
    k = kv[:, :HD]
    v = kv[:, HD:]
    s = lax.dot_general(q, k, NT, preferred_element_type=jnp.float32) * scale
    top = jnp.max(s, axis=1, keepdims=True)
    e = jnp.exp(s - top)
    p = e / jnp.sum(e, axis=1, keepdims=True)
    if valid is not None:
        p = jnp.where(valid, p, 0.0)
    p_low = p.astype(jnp.bfloat16)
    att = jnp.dot(p_low, v, preferred_element_type=jnp.float32)
    gp = lax.dot_general(g, v, NT, preferred_element_type=jnp.float32)
    delta = jnp.sum(p * gp, axis=1, keepdims=True)
    gs = (p * (gp - delta) * scale).astype(jnp.bfloat16)
    gq = jnp.dot(gs, k, preferred_element_type=jnp.float32)
    dk = lax.dot_general(gs, q, TN, preferred_element_type=jnp.float32)
    dv = lax.dot_general(p_low, g, TN, preferred_element_type=jnp.float32)
    dkv = jnp.concatenate([dk, dv], axis=1)
    for t, u in enumerate(units):
        acc_ref[u] += dkv[SPAN * t:SPAN * (t + 1)]
    return jnp.concatenate([att, gq], axis=1)


def _kernel(unroll, nb_ref, qg_ref, kv_ref, out_ref, acc_ref):
    pieces = qg_ref.shape[0]
    acc_ref[...] = jnp.zeros(acc_ref.shape, acc_ref.dtype)
    scale = 1.0 / math.sqrt(HD)
    rows = qg_ref.shape[2]
    row = lax.broadcasted_iota(jnp.int32, (rows, 1), 0)
    head = row == 0

    def even(piece, carry):
        out = _span(qg_ref[piece, 0], kv_ref, acc_ref, nb_ref, 2 * piece, None, scale)
        out_ref[piece, 0] = out.astype(out_ref.dtype)
        return carry

    def odd(piece, carry):
        prev = (piece + pieces - 1) % pieces
        tile = jnp.where(
            head, qg_ref[prev, 1].astype(jnp.float32), qg_ref[piece, 1].astype(jnp.float32)
        ).astype(jnp.bfloat16)
        span = (2 * piece + 2 * pieces - 1) % (2 * pieces)
        valid = head | (piece >= 1)
        out = _span(tile, kv_ref, acc_ref, nb_ref, span, valid, scale)
        mine = out_ref[piece, 1].astype(jnp.float32)
        out_ref[piece, 1] = jnp.where(head, mine, out).astype(out_ref.dtype)
        before = out_ref[prev, 1].astype(jnp.float32)
        out_ref[prev, 1] = jnp.where(head, out, before).astype(out_ref.dtype)
        return carry

    lax.fori_loop(0, pieces, even, 0, unroll=unroll)
    lax.fori_loop(0, pieces, odd, 0, unroll=unroll)


def attend(nb, qg, kv, unroll=2):
    pieces, chunks, rows, lanes = qg.shape
    units = kv.shape[0]
    whole_qg = pl.BlockSpec(qg.shape, lambda j, nb: (0, 0, 0, 0))
    whole_kv = pl.BlockSpec(kv.shape, lambda j, nb: (0, 0, 0))
    acc_shape = (units, SPAN, 2 * HD)
    whole_acc = pl.BlockSpec(acc_shape, lambda j, nb: (0, 0, 0))
    flops = pieces * chunks * rows * 4 * SPAN * HD * 2 * 6
    bytes_accessed = 2 * qg.size * 2 + kv.size * 2 + math.prod(acc_shape) * 4
    call = pl.pallas_call(
        functools.partial(_kernel, unroll),
        grid_spec=pltpu.PrefetchScalarGridSpec(
            num_scalar_prefetch=1,
            grid=(1,),
            in_specs=[whole_qg, whole_kv],
            out_specs=[whole_qg, whole_acc],
        ),
        out_shape=[
            jax.ShapeDtypeStruct(qg.shape, jnp.bfloat16),
            jax.ShapeDtypeStruct(acc_shape, jnp.float32),
        ],
        compiler_params=pltpu.CompilerParams(
            dimension_semantics=("arbitrary",), vmem_limit_bytes=56 * 1024 * 1024
        ),
        cost_estimate=pl.CostEstimate(
            flops=flops, transcendentals=pieces * chunks * rows * 4 * SPAN, bytes_accessed=bytes_accessed
        ),
        name="attend",
    )
    return call(nb, qg, kv)


def local(queries, cotangent, states, neighbours):
    parts = lax.axis_size("seq")
    groups = lax.axis_size("dp")
    tok_dev = queries.shape[1]
    width = queries.shape[2]
    heads = width // HD
    quarter = SPAN // groups
    member = lax.axis_index("dp")

    st = states.reshape(SPAN, 2, heads, HD)
    st = lax.dynamic_slice_in_dim(st, member * quarter, quarter, axis=0)[None]
    moved = lax.all_to_all(st, "seq", split_axis=3, concat_axis=0, tiled=True)
    kv = lax.all_gather(moved, "dp", axis=1, tiled=True).reshape(parts, SPAN, 2 * HD)
    nb = neighbours.reshape(-1)

    both = jnp.stack(
        [queries.reshape(tok_dev, heads, HD), cotangent.reshape(tok_dev, heads, HD)], axis=2
    )
    lead = SPAN - 1
    chunks = (
        both[lead:lead + SPAN],
        jnp.concatenate([both[tok_dev - 1:], both[:lead]], axis=0),
    )
    part = jnp.stack(chunks, axis=0)
    qg = lax.all_to_all(part, "seq", split_axis=2, concat_axis=0, tiled=True)
    out, acc = attend(nb, qg.reshape(parts, 2, SPAN, 2 * HD), kv)
    out = lax.all_to_all(
        out.reshape(parts, 2, SPAN, 1, 2, HD), "seq", split_axis=0, concat_axis=3, tiled=True
    ).reshape(2, SPAN, heads, 2, HD)
    rows = jnp.concatenate([out[1, 1:], out[0], out[1, :1]], axis=0)
    attended = rows[:, :, 0].reshape(1, tok_dev, width)
    query_grad = rows[:, :, 1].reshape(1, tok_dev, width)

    red = lax.psum_scatter(acc, "dp", scatter_dimension=1, tiled=True).astype(jnp.bfloat16)
    home = lax.all_to_all(red, "seq", split_axis=0, concat_axis=0, tiled=True)
    home = home.reshape(heads, quarter, 2, HD).transpose(1, 2, 0, 3).reshape(quarter, 2 * width)
    state_grad = lax.all_gather(home, "dp", axis=0, tiled=True).reshape(1, SPAN, 2 * width)
    return (attended, query_grad, state_grad)


def solution(mesh):
    placed = (P("dp", "seq", None), P("dp", "seq", None), P("seq", None, None), P("dp", None, None))
    return jax.shard_map(
        local,
        mesh=mesh,
        in_specs=placed,
        out_specs=(P("dp", "seq", None), P("dp", "seq", None), P("seq", None, None)),
        check_vma=False,
    )
```

```python
import functools
import math

import jax
import jax.numpy as jnp
from jax import lax
from jax.experimental import pallas as pl
from jax.experimental.pallas import tpu as pltpu
from jax.sharding import PartitionSpec as P

SPAN = 64
HD = 128
NT = (((1,), (1,)), ((), ()))
TN = (((0,), (0,)), ((), ()))


def _span(qg, kv_ref, acc_ref, nb_ref, span, valid, scale):
    q = qg[:, :HD]
    g = qg[:, HD:]
    u0 = nb_ref[2 * span]
    u1 = nb_ref[2 * span + 1]
    units = (u0, u0 + 1, u1, u1 + 1)
    kv = jnp.concatenate([kv_ref[u] for u in units], axis=0)
    k = kv[:, :HD]
    v = kv[:, HD:]
    s = lax.dot_general(q, k, NT, preferred_element_type=jnp.float32) * scale
    top = jnp.max(s, axis=1, keepdims=True)
    e = jnp.exp(s - top)
    p = e / jnp.sum(e, axis=1, keepdims=True)
    if valid is not None:
        p = jnp.where(valid, p, 0.0)
    p_low = p.astype(jnp.bfloat16)
    att = jnp.dot(p_low, v, preferred_element_type=jnp.float32)
    gp = lax.dot_general(g, v, NT, preferred_element_type=jnp.float32)
    delta = jnp.sum(p * gp, axis=1, keepdims=True)
    gs = (p * (gp - delta) * scale).astype(jnp.bfloat16)
    gq = jnp.dot(gs, k, preferred_element_type=jnp.float32)
    dk = lax.dot_general(gs, q, TN, preferred_element_type=jnp.float32)
    dv = lax.dot_general(p_low, g, TN, preferred_element_type=jnp.float32)
    dkv = jnp.concatenate([dk, dv], axis=1)
    for t, u in enumerate(units):
        acc_ref[u] += dkv[SPAN * t:SPAN * (t + 1)]
    return jnp.concatenate([att, gq], axis=1)


def _kernel(unroll, nb_ref, qg0_ref, qg1_ref, kv_ref, out0_ref, out1_ref, acc_ref):
    pieces = qg0_ref.shape[0]
    acc_ref[...] = jnp.zeros(acc_ref.shape, acc_ref.dtype)
    scale = 1.0 / math.sqrt(HD)
    rows = qg0_ref.shape[1]
    row = lax.broadcasted_iota(jnp.int32, (rows, 1), 0)
    head = row == 0

    def even(piece, carry):
        out = _span(qg0_ref[piece], kv_ref, acc_ref, nb_ref, 2 * piece, None, scale)
        out0_ref[piece] = out.astype(out0_ref.dtype)
        return carry

    def odd(piece, carry):
        prev = (piece + pieces - 1) % pieces
        tile = jnp.where(
            head, qg1_ref[prev].astype(jnp.float32), qg1_ref[piece].astype(jnp.float32)
        ).astype(jnp.bfloat16)
        span = (2 * piece + 2 * pieces - 1) % (2 * pieces)
        valid = head | (piece >= 1)
        out = _span(tile, kv_ref, acc_ref, nb_ref, span, valid, scale)
        mine = out1_ref[piece].astype(jnp.float32)
        out1_ref[piece] = jnp.where(head, mine, out).astype(out1_ref.dtype)
        before = out1_ref[prev].astype(jnp.float32)
        out1_ref[prev] = jnp.where(head, out, before).astype(out1_ref.dtype)
        return carry

    lax.fori_loop(0, pieces, even, 0, unroll=unroll)
    lax.fori_loop(0, pieces, odd, 0, unroll=unroll)


def attend(nb, qg0, qg1, kv, unroll=2):
    pieces, rows, lanes = qg0.shape
    units = kv.shape[0]
    whole_qg = pl.BlockSpec(qg0.shape, lambda j, nb: (0, 0, 0))
    whole_kv = pl.BlockSpec(kv.shape, lambda j, nb: (0, 0, 0))
    acc_shape = (units, SPAN, 2 * HD)
    whole_acc = pl.BlockSpec(acc_shape, lambda j, nb: (0, 0, 0))
    flops = 2 * pieces * rows * 4 * SPAN * HD * 2 * 6
    bytes_accessed = 4 * qg0.size * 2 + kv.size * 2 + math.prod(acc_shape) * 4
    call = pl.pallas_call(
        functools.partial(_kernel, unroll),
        grid_spec=pltpu.PrefetchScalarGridSpec(
            num_scalar_prefetch=1,
            grid=(1,),
            in_specs=[whole_qg, whole_qg, whole_kv],
            out_specs=[whole_qg, whole_qg, whole_acc],
        ),
        out_shape=[
            jax.ShapeDtypeStruct(qg0.shape, jnp.bfloat16),
            jax.ShapeDtypeStruct(qg0.shape, jnp.bfloat16),
            jax.ShapeDtypeStruct(acc_shape, jnp.float32),
        ],
        compiler_params=pltpu.CompilerParams(
            dimension_semantics=("arbitrary",), vmem_limit_bytes=56 * 1024 * 1024
        ),
        cost_estimate=pl.CostEstimate(
            flops=flops, transcendentals=2 * pieces * rows * 4 * SPAN, bytes_accessed=bytes_accessed
        ),
        name="attend",
    )
    return call(nb, qg0, qg1, kv)


def local(queries, cotangent, states, neighbours):
    parts = lax.axis_size("seq")
    groups = lax.axis_size("dp")
    tok_dev = queries.shape[1]
    width = queries.shape[2]
    heads = width // HD
    quarter = SPAN // groups
    member = lax.axis_index("dp")

    st = states.reshape(SPAN, 2, heads, HD)
    st = lax.dynamic_slice_in_dim(st, member * quarter, quarter, axis=0)[None]
    moved = lax.all_to_all(st, "seq", split_axis=3, concat_axis=0, tiled=True)
    kv = lax.all_gather(moved, "dp", axis=1, tiled=True).reshape(parts, SPAN, 2 * HD)
    nb = neighbours.reshape(-1)

    both = jnp.stack(
        [queries.reshape(tok_dev, heads, HD), cotangent.reshape(tok_dev, heads, HD)], axis=2
    )
    lead = SPAN - 1
    chunks = (
        both[lead:lead + SPAN],
        jnp.concatenate([both[tok_dev - 1:], both[:lead]], axis=0),
    )
    qgs = [
        lax.all_to_all(part, "seq", split_axis=1, concat_axis=0, tiled=True).reshape(
            parts, SPAN, 2 * HD
        )
        for part in chunks
    ]
    out0, out1, acc = attend(nb, qgs[0], qgs[1], kv)
    red = lax.psum_scatter(acc.astype(jnp.bfloat16), "dp", scatter_dimension=1, tiled=True)
    outs = [
        lax.all_to_all(
            out.reshape(parts, SPAN, 1, 2, HD), "seq", split_axis=0, concat_axis=2, tiled=True
        ).reshape(SPAN, heads, 2, HD)
        for out in (out0, out1)
    ]
    red, outs = lax.optimization_barrier((red, outs))
    rows = jnp.concatenate([outs[1][1:], outs[0], outs[1][:1]], axis=0)
    attended = rows[:, :, 0].reshape(1, tok_dev, width)
    query_grad = rows[:, :, 1].reshape(1, tok_dev, width)

    home = lax.all_to_all(red, "seq", split_axis=0, concat_axis=0, tiled=True)
    home = home.reshape(heads, quarter, 2, HD).transpose(1, 2, 0, 3).reshape(quarter, 2 * width)
    state_grad = lax.all_gather(home, "dp", axis=0, tiled=True).reshape(1, SPAN, 2 * width)
    return (attended, query_grad, state_grad)


def solution(mesh):
    placed = (P("dp", "seq", None), P("dp", "seq", None), P("seq", None, None), P("dp", None, None))
    return jax.shard_map(
        local,
        mesh=mesh,
        in_specs=placed,
        out_specs=(P("dp", "seq", None), P("dp", "seq", None), P("seq", None, None)),
        check_vma=False,
    )
```

```python
import functools
import math

import jax
import jax.numpy as jnp
from jax import lax
from jax.experimental import pallas as pl
from jax.experimental.pallas import tpu as pltpu
from jax.sharding import PartitionSpec as P

SPAN = 64
HD = 128
NT = (((1,), (1,)), ((), ()))
TN = (((0,), (0,)), ((), ()))


def _span(qg, kv_ref, acc_ref, nb_ref, span, valid, scale):
    q = qg[:, :HD]
    g = qg[:, HD:]
    u0 = nb_ref[2 * span]
    u1 = nb_ref[2 * span + 1]
    units = (u0, u0 + 1, u1, u1 + 1)
    kv = jnp.concatenate([kv_ref[u] for u in units], axis=0)
    k = kv[:, :HD]
    v = kv[:, HD:]
    s = lax.dot_general(q, k, NT, preferred_element_type=jnp.float32) * scale
    top = jnp.max(s, axis=1, keepdims=True)
    e = jnp.exp(s - top)
    p = e / jnp.sum(e, axis=1, keepdims=True)
    if valid is not None:
        p = jnp.where(valid, p, 0.0)
    p_low = p.astype(jnp.bfloat16)
    att = jnp.dot(p_low, v, preferred_element_type=jnp.float32)
    gp = lax.dot_general(g, v, NT, preferred_element_type=jnp.float32)
    delta = jnp.sum(p * gp, axis=1, keepdims=True)
    gs = (p * (gp - delta) * scale).astype(jnp.bfloat16)
    gq = jnp.dot(gs, k, preferred_element_type=jnp.float32)
    dk = lax.dot_general(gs, q, TN, preferred_element_type=jnp.float32)
    dv = lax.dot_general(p_low, g, TN, preferred_element_type=jnp.float32)
    dkv = jnp.concatenate([dk, dv], axis=1)
    for t, u in enumerate(units):
        acc_ref[u] += dkv[SPAN * t:SPAN * (t + 1)]
    return jnp.concatenate([att, gq], axis=1)


def _kernel(unroll, nb_ref, qg0_ref, qg1_ref, kv_ref, out0_ref, out1_ref, acc_ref):
    pieces = qg0_ref.shape[0]
    acc_ref[...] = jnp.zeros(acc_ref.shape, acc_ref.dtype)
    scale = 1.0 / math.sqrt(HD)
    rows = qg0_ref.shape[1]
    row = lax.broadcasted_iota(jnp.int32, (rows, 1), 0)
    head = row == 0

    def even(piece, carry):
        out = _span(qg0_ref[piece], kv_ref, acc_ref, nb_ref, 2 * piece, None, scale)
        out0_ref[piece] = out.astype(out0_ref.dtype)
        return carry

    def odd(piece, carry):
        prev = (piece + pieces - 1) % pieces
        tile = jnp.where(
            head, qg1_ref[prev].astype(jnp.float32), qg1_ref[piece].astype(jnp.float32)
        ).astype(jnp.bfloat16)
        span = (2 * piece + 2 * pieces - 1) % (2 * pieces)
        valid = head | (piece >= 1)
        out = _span(tile, kv_ref, acc_ref, nb_ref, span, valid, scale)
        mine = out1_ref[piece].astype(jnp.float32)
        out1_ref[piece] = jnp.where(head, mine, out).astype(out1_ref.dtype)
        before = out1_ref[prev].astype(jnp.float32)
        out1_ref[prev] = jnp.where(head, out, before).astype(out1_ref.dtype)
        return carry

    lax.fori_loop(0, pieces, even, 0, unroll=unroll)
    lax.fori_loop(0, pieces, odd, 0, unroll=unroll)


def attend(nb, qg0, qg1, kv, unroll=4):
    pieces, rows, lanes = qg0.shape
    units = kv.shape[0]
    whole_qg = pl.BlockSpec(qg0.shape, lambda j, nb: (0, 0, 0))
    whole_kv = pl.BlockSpec(kv.shape, lambda j, nb: (0, 0, 0))
    acc_shape = (units, SPAN, 2 * HD)
    whole_acc = pl.BlockSpec(acc_shape, lambda j, nb: (0, 0, 0))
    flops = 2 * pieces * rows * 4 * SPAN * HD * 2 * 6
    bytes_accessed = 4 * qg0.size * 2 + kv.size * 2 + math.prod(acc_shape) * 4
    call = pl.pallas_call(
        functools.partial(_kernel, unroll),
        grid_spec=pltpu.PrefetchScalarGridSpec(
            num_scalar_prefetch=1,
            grid=(1,),
            in_specs=[whole_qg, whole_qg, whole_kv],
            out_specs=[whole_qg, whole_qg, whole_acc],
        ),
        out_shape=[
            jax.ShapeDtypeStruct(qg0.shape, jnp.bfloat16),
            jax.ShapeDtypeStruct(qg0.shape, jnp.bfloat16),
            jax.ShapeDtypeStruct(acc_shape, jnp.float32),
        ],
        compiler_params=pltpu.CompilerParams(
            dimension_semantics=("arbitrary",), vmem_limit_bytes=56 * 1024 * 1024
        ),
        cost_estimate=pl.CostEstimate(
            flops=flops, transcendentals=2 * pieces * rows * 4 * SPAN, bytes_accessed=bytes_accessed
        ),
        name="attend",
    )
    return call(nb, qg0, qg1, kv)


def local(queries, cotangent, states, neighbours):
    parts = lax.axis_size("seq")
    groups = lax.axis_size("dp")
    tok_dev = queries.shape[1]
    width = queries.shape[2]
    heads = width // HD
    quarter = SPAN // groups
    member = lax.axis_index("dp")

    st = states.reshape(SPAN, 2, heads, HD)
    st = lax.dynamic_slice_in_dim(st, member * quarter, quarter, axis=0)[None]
    moved = lax.all_to_all(st, "seq", split_axis=3, concat_axis=0, tiled=True)
    kv = lax.all_gather(moved, "dp", axis=1, tiled=True).reshape(parts, SPAN, 2 * HD)
    nb = neighbours.reshape(-1)

    both = jnp.stack(
        [queries.reshape(tok_dev, heads, HD), cotangent.reshape(tok_dev, heads, HD)], axis=2
    )
    lead = SPAN - 1
    chunks = (
        both[lead:lead + SPAN],
        jnp.concatenate([both[tok_dev - 1:], both[:lead]], axis=0),
    )
    qgs = [
        lax.all_to_all(part, "seq", split_axis=1, concat_axis=0, tiled=True).reshape(
            parts, SPAN, 2 * HD
        )
        for part in chunks
    ]
    out0, out1, acc = attend(nb, qgs[0], qgs[1], kv)
    red = lax.psum_scatter(acc.astype(jnp.bfloat16), "dp", scatter_dimension=1, tiled=True)
    outs = [
        lax.all_to_all(
            out.reshape(parts, SPAN, 1, 2, HD), "seq", split_axis=0, concat_axis=2, tiled=True
        ).reshape(SPAN, heads, 2, HD)
        for out in (out0, out1)
    ]
    rows = jnp.concatenate([outs[1][1:], outs[0], outs[1][:1]], axis=0)
    attended = rows[:, :, 0].reshape(1, tok_dev, width)
    query_grad = rows[:, :, 1].reshape(1, tok_dev, width)

    home = lax.all_to_all(red, "seq", split_axis=0, concat_axis=0, tiled=True)
    home = home.reshape(heads, quarter, 2, HD).transpose(1, 2, 0, 3).reshape(quarter, 2 * width)
    state_grad = lax.all_gather(home, "dp", axis=0, tiled=True).reshape(1, SPAN, 2 * width)
    return (attended, query_grad, state_grad)


def solution(mesh):
    placed = (P("dp", "seq", None), P("dp", "seq", None), P("seq", None, None), P("dp", None, None))
    return jax.shard_map(
        local,
        mesh=mesh,
        in_specs=placed,
        out_specs=(P("dp", "seq", None), P("dp", "seq", None), P("seq", None, None)),
        check_vma=False,
    )
```

```python
import functools
import math

import jax
import jax.numpy as jnp
from jax import lax
from jax.experimental import pallas as pl
from jax.experimental.pallas import tpu as pltpu
from jax.sharding import PartitionSpec as P

SPAN = 64
HD = 128
NT = (((1,), (1,)), ((), ()))
TN = (((0,), (0,)), ((), ()))


def _span(q, g, kv_ref, acc_ref, nb_ref, span, valid, scale):
    u0 = nb_ref[2 * span]
    u1 = nb_ref[2 * span + 1]
    units = (u0, u0 + 1, u1, u1 + 1)
    kv = jnp.concatenate([kv_ref[u] for u in units], axis=0)
    k = kv[:, :HD]
    v = kv[:, HD:]
    s = lax.dot_general(q, k, NT, preferred_element_type=jnp.float32) * scale
    top = jnp.max(s, axis=1, keepdims=True)
    e = jnp.exp(s - top)
    p = e / jnp.sum(e, axis=1, keepdims=True)
    if valid is not None:
        p = jnp.where(valid, p, 0.0)
    p_low = p.astype(jnp.bfloat16)
    att = jnp.dot(p_low, v, preferred_element_type=jnp.float32)
    gp = lax.dot_general(g, v, NT, preferred_element_type=jnp.float32)
    delta = jnp.sum(p * gp, axis=1, keepdims=True)
    gs = (p * (gp - delta) * scale).astype(jnp.bfloat16)
    gq = jnp.dot(gs, k, preferred_element_type=jnp.float32)
    dk = lax.dot_general(gs, q, TN, preferred_element_type=jnp.float32)
    dv = lax.dot_general(p_low, g, TN, preferred_element_type=jnp.float32)
    dkv = jnp.concatenate([dk, dv], axis=1)
    for t, u in enumerate(units):
        acc_ref[u] += dkv[SPAN * t:SPAN * (t + 1)]
    return att, gq


def _kernel(unroll, nb_ref, q_ref, g_ref, kv_ref, att_ref, gq_ref, acc_ref):
    pieces = q_ref.shape[0]
    acc_ref[...] = jnp.zeros(acc_ref.shape, acc_ref.dtype)
    scale = 1.0 / math.sqrt(HD)
    row = lax.broadcasted_iota(jnp.int32, (SPAN, 1), 0)
    first = row == 0
    last = row == SPAN - 1
    down = lambda x: pltpu.roll(x, 1, 0)
    up = lambda x: pltpu.roll(x, SPAN - 1, 0)
    lo = pl.ds(0, SPAN)
    hi = pl.ds(SPAN, SPAN)

    def tiles(ref, piece, prev):
        a = down(ref[piece, lo, :].astype(jnp.float32))
        b = down(ref[piece, hi, :].astype(jnp.float32))
        c = down(ref[prev, hi, :].astype(jnp.float32))
        even = jnp.where(first, a, b).astype(jnp.bfloat16)
        odd = jnp.where(first, c, a).astype(jnp.bfloat16)
        return even, odd

    def put(ref, piece, prev, even, odd):
        e = up(even)
        o = up(odd)
        ref[piece, lo, :] = jnp.where(last, e, o).astype(ref.dtype)
        kept = ref[piece, hi, :].astype(jnp.float32)
        ref[piece, hi, :] = jnp.where(last, kept, e).astype(ref.dtype)
        before = ref[prev, hi, :].astype(jnp.float32)
        ref[prev, hi, :] = jnp.where(last, o, before).astype(ref.dtype)

    def body(piece, carry):
        prev = (piece + pieces - 1) % pieces
        q_even, q_odd = tiles(q_ref, piece, prev)
        g_even, g_odd = tiles(g_ref, piece, prev)
        att_e, gq_e = _span(q_even, g_even, kv_ref, acc_ref, nb_ref, 2 * piece, None, scale)
        odd_span = (2 * piece + 2 * pieces - 1) % (2 * pieces)
        valid = first | (piece >= 1)
        att_o, gq_o = _span(q_odd, g_odd, kv_ref, acc_ref, nb_ref, odd_span, valid, scale)
        put(att_ref, piece, prev, att_e, att_o)
        put(gq_ref, piece, prev, gq_e, gq_o)
        return carry

    lax.fori_loop(0, pieces, body, 0, unroll=unroll)


def attend(nb, q, g, kv, unroll=4):
    pieces, rows, lanes = q.shape
    units = kv.shape[0]
    whole_q = pl.BlockSpec(q.shape, lambda j, nb: (0, 0, 0))
    whole_kv = pl.BlockSpec(kv.shape, lambda j, nb: (0, 0, 0))
    acc_shape = (units, SPAN, 2 * HD)
    whole_acc = pl.BlockSpec(acc_shape, lambda j, nb: (0, 0, 0))
    flops = pieces * rows * 4 * SPAN * HD * 2 * 6
    bytes_accessed = 4 * q.size * 2 + kv.size * 2 + math.prod(acc_shape) * 4
    call = pl.pallas_call(
        functools.partial(_kernel, unroll),
        grid_spec=pltpu.PrefetchScalarGridSpec(
            num_scalar_prefetch=1,
            grid=(1,),
            in_specs=[whole_q, whole_q, whole_kv],
            out_specs=[whole_q, whole_q, whole_acc],
        ),
        out_shape=[
            jax.ShapeDtypeStruct(q.shape, jnp.bfloat16),
            jax.ShapeDtypeStruct(q.shape, jnp.bfloat16),
            jax.ShapeDtypeStruct(acc_shape, jnp.float32),
        ],
        compiler_params=pltpu.CompilerParams(
            dimension_semantics=("arbitrary",), vmem_limit_bytes=56 * 1024 * 1024
        ),
        cost_estimate=pl.CostEstimate(
            flops=flops, transcendentals=pieces * rows * 4 * SPAN, bytes_accessed=bytes_accessed
        ),
        name="attend",
    )
    return call(nb, q, g, kv)


def local(queries, cotangent, states, neighbours):
    parts = lax.axis_size("seq")
    groups = lax.axis_size("dp")
    tok_dev = queries.shape[1]
    width = queries.shape[2]
    heads = width // HD
    quarter = SPAN // groups
    member = lax.axis_index("dp")

    st = states.reshape(SPAN, 2, heads, HD)
    st = lax.dynamic_slice_in_dim(st, member * quarter, quarter, axis=0)[None]
    moved = lax.all_to_all(st, "seq", split_axis=3, concat_axis=0, tiled=True)
    kv = lax.all_gather(moved, "dp", axis=1, tiled=True).reshape(parts, SPAN, 2 * HD)
    nb = neighbours.reshape(-1)

    def heads_in(x):
        x = lax.all_to_all(x.reshape(tok_dev, heads, HD), "seq", split_axis=1, concat_axis=0, tiled=True)
        return x.reshape(parts, tok_dev, HD)

    def heads_out(x):
        x = lax.all_to_all(x.reshape(parts, tok_dev, 1, HD), "seq", split_axis=0, concat_axis=2, tiled=True)
        return x.reshape(1, tok_dev, width)

    att, gq, acc = attend(nb, heads_in(queries), heads_in(cotangent), kv)
    red = lax.psum_scatter(acc.astype(jnp.bfloat16), "dp", scatter_dimension=1, tiled=True)
    attended = heads_out(att)
    query_grad = heads_out(gq)

    home = lax.all_to_all(red, "seq", split_axis=0, concat_axis=0, tiled=True)
    home = home.reshape(heads, quarter, 2, HD).transpose(1, 2, 0, 3).reshape(quarter, 2 * width)
    state_grad = lax.all_gather(home, "dp", axis=0, tiled=True).reshape(1, SPAN, 2 * width)
    return (attended, query_grad, state_grad)


def solution(mesh):
    placed = (P("dp", "seq", None), P("dp", "seq", None), P("seq", None, None), P("dp", None, None))
    return jax.shard_map(
        local,
        mesh=mesh,
        in_specs=placed,
        out_specs=(P("dp", "seq", None), P("dp", "seq", None), P("seq", None, None)),
        check_vma=False,
    )
```

```python
import functools
import math

import jax
import jax.numpy as jnp
from jax import lax
from jax.experimental import pallas as pl
from jax.experimental.pallas import tpu as pltpu
from jax.sharding import PartitionSpec as P

SPAN = 64
HD = 128
NT = (((1,), (1,)), ((), ()))
TN = (((0,), (0,)), ((), ()))


def _span(q, g, kv_ref, acc_ref, nb_ref, span, valid, scale):
    u0 = nb_ref[2 * span]
    u1 = nb_ref[2 * span + 1]
    units = (u0, u0 + 1, u1, u1 + 1)
    kv = jnp.concatenate([kv_ref[u] for u in units], axis=0)
    k = kv[:, :HD]
    v = kv[:, HD:]
    s = lax.dot_general(q, k, NT, preferred_element_type=jnp.float32) * scale
    top = jnp.max(s, axis=1, keepdims=True)
    e = jnp.exp(s - top)
    p = e / jnp.sum(e, axis=1, keepdims=True)
    if valid is not None:
        p = jnp.where(valid, p, 0.0)
    p_low = p.astype(jnp.bfloat16)
    att = jnp.dot(p_low, v, preferred_element_type=jnp.float32)
    gp = lax.dot_general(g, v, NT, preferred_element_type=jnp.float32)
    delta = jnp.sum(p * gp, axis=1, keepdims=True)
    gs = (p * (gp - delta) * scale).astype(jnp.bfloat16)
    gq = jnp.dot(gs, k, preferred_element_type=jnp.float32)
    dk = lax.dot_general(gs, q, TN, preferred_element_type=jnp.float32)
    dv = lax.dot_general(p_low, g, TN, preferred_element_type=jnp.float32)
    dkv = jnp.concatenate([dk, dv], axis=1)
    for t, u in enumerate(units):
        acc_ref[u] += dkv[SPAN * t:SPAN * (t + 1)]
    return att, gq


def _kernel(unroll, nb_ref, q_ref, g_ref, kv_ref, att_ref, gq_ref, grad_ref, acc_ref):
    pieces = q_ref.shape[0]
    acc_ref[...] = jnp.zeros(acc_ref.shape, acc_ref.dtype)
    scale = 1.0 / math.sqrt(HD)
    row = lax.broadcasted_iota(jnp.int32, (SPAN, 1), 0)
    first = row == 0
    last = row == SPAN - 1
    down = lambda x: pltpu.roll(x, 1, 0)
    up = lambda x: pltpu.roll(x, SPAN - 1, 0)
    lo = pl.ds(0, SPAN)
    hi = pl.ds(SPAN, SPAN)

    def tiles(ref, piece, prev):
        a = down(ref[piece, lo, :].astype(jnp.float32))
        b = down(ref[piece, hi, :].astype(jnp.float32))
        c = down(ref[prev, hi, :].astype(jnp.float32))
        even = jnp.where(first, a, b).astype(jnp.bfloat16)
        odd = jnp.where(first, c, a).astype(jnp.bfloat16)
        return even, odd

    def put(ref, piece, prev, even, odd):
        e = up(even)
        o = up(odd)
        ref[piece, lo, :] = jnp.where(last, e, o).astype(ref.dtype)
        kept = ref[piece, hi, :].astype(jnp.float32)
        ref[piece, hi, :] = jnp.where(last, kept, e).astype(ref.dtype)
        before = ref[prev, hi, :].astype(jnp.float32)
        ref[prev, hi, :] = jnp.where(last, o, before).astype(ref.dtype)

    def body(piece, carry):
        prev = (piece + pieces - 1) % pieces
        q_even, q_odd = tiles(q_ref, piece, prev)
        g_even, g_odd = tiles(g_ref, piece, prev)
        att_e, gq_e = _span(q_even, g_even, kv_ref, acc_ref, nb_ref, 2 * piece, None, scale)
        odd_span = (2 * piece + 2 * pieces - 1) % (2 * pieces)
        valid = first | (piece >= 1)
        att_o, gq_o = _span(q_odd, g_odd, kv_ref, acc_ref, nb_ref, odd_span, valid, scale)
        put(att_ref, piece, prev, att_e, att_o)
        put(gq_ref, piece, prev, gq_e, gq_o)
        return carry

    lax.fori_loop(0, pieces, body, 0, unroll=unroll)
    grad_ref[...] = acc_ref[...].astype(grad_ref.dtype)


def attend(nb, q, g, kv, unroll=8):
    pieces, rows, lanes = q.shape
    units = kv.shape[0]
    whole_q = pl.BlockSpec(q.shape, lambda j, nb: (0, 0, 0))
    whole_kv = pl.BlockSpec(kv.shape, lambda j, nb: (0, 0, 0))
    acc_shape = (units, SPAN, 2 * HD)
    whole_acc = pl.BlockSpec(acc_shape, lambda j, nb: (0, 0, 0))
    flops = pieces * rows * 4 * SPAN * HD * 2 * 6
    bytes_accessed = 4 * q.size * 2 + kv.size * 2 + math.prod(acc_shape) * 2
    call = pl.pallas_call(
        functools.partial(_kernel, unroll),
        grid_spec=pltpu.PrefetchScalarGridSpec(
            num_scalar_prefetch=1,
            grid=(1,),
            in_specs=[whole_q, whole_q, whole_kv],
            out_specs=[whole_q, whole_q, whole_acc],
            scratch_shapes=[pltpu.VMEM(acc_shape, jnp.float32)],
        ),
        out_shape=[
            jax.ShapeDtypeStruct(q.shape, jnp.bfloat16),
            jax.ShapeDtypeStruct(q.shape, jnp.bfloat16),
            jax.ShapeDtypeStruct(acc_shape, jnp.bfloat16),
        ],
        compiler_params=pltpu.CompilerParams(
            dimension_semantics=("arbitrary",), vmem_limit_bytes=56 * 1024 * 1024
        ),
        cost_estimate=pl.CostEstimate(
            flops=flops, transcendentals=pieces * rows * 4 * SPAN, bytes_accessed=bytes_accessed
        ),
        name="attend",
    )
    return call(nb, q, g, kv)


def local(queries, cotangent, states, neighbours):
    parts = lax.axis_size("seq")
    groups = lax.axis_size("dp")
    tok_dev = queries.shape[1]
    width = queries.shape[2]
    heads = width // HD
    quarter = SPAN // groups
    member = lax.axis_index("dp")

    st = states.reshape(SPAN, 2, heads, HD)
    st = lax.dynamic_slice_in_dim(st, member * quarter, quarter, axis=0)[None]
    moved = lax.all_to_all(st, "seq", split_axis=3, concat_axis=0, tiled=True)
    kv = lax.all_gather(moved, "dp", axis=1, tiled=True).reshape(parts, SPAN, 2 * HD)
    nb = neighbours.reshape(-1)

    def heads_in(x):
        x = lax.all_to_all(x.reshape(tok_dev, heads, HD), "seq", split_axis=1, concat_axis=0, tiled=True)
        return x.reshape(parts, tok_dev, HD)

    def heads_out(x):
        x = lax.all_to_all(x.reshape(parts, tok_dev, 1, HD), "seq", split_axis=0, concat_axis=2, tiled=True)
        return x.reshape(1, tok_dev, width)

    att, gq, acc = attend(nb, heads_in(queries), heads_in(cotangent), kv)
    red = lax.psum_scatter(acc, "dp", scatter_dimension=1, tiled=True)
    attended = heads_out(att)
    query_grad = heads_out(gq)

    home = lax.all_to_all(red, "seq", split_axis=0, concat_axis=0, tiled=True)
    home = home.reshape(heads, quarter, 2, HD).transpose(1, 2, 0, 3).reshape(quarter, 2 * width)
    state_grad = lax.all_gather(home, "dp", axis=0, tiled=True).reshape(1, SPAN, 2 * width)
    return (attended, query_grad, state_grad)


def solution(mesh):
    placed = (P("dp", "seq", None), P("dp", "seq", None), P("seq", None, None), P("dp", None, None))
    return jax.shard_map(
        local,
        mesh=mesh,
        in_specs=placed,
        out_specs=(P("dp", "seq", None), P("dp", "seq", None), P("seq", None, None)),
        check_vma=False,
    )
```

```python
import functools
import math

import jax
import jax.numpy as jnp
from jax import lax
from jax.experimental import pallas as pl
from jax.experimental.pallas import tpu as pltpu
from jax.sharding import PartitionSpec as P

SPAN = 64
HD = 128
NT = (((1,), (1,)), ((), ()))
TN = (((0,), (0,)), ((), ()))


def _span(q, g, kv_ref, acc_ref, nb_ref, span, valid, scale):
    u0 = nb_ref[2 * span]
    u1 = nb_ref[2 * span + 1]
    units = (u0, u0 + 1, u1, u1 + 1)
    kv = jnp.concatenate([kv_ref[u] for u in units], axis=0)
    k = kv[:, :HD]
    v = kv[:, HD:]
    s = lax.dot_general(q, k, NT, preferred_element_type=jnp.float32) * scale
    top = jnp.max(s, axis=1, keepdims=True)
    e = jnp.exp(s - top)
    p = e / jnp.sum(e, axis=1, keepdims=True)
    if valid is not None:
        p = jnp.where(valid, p, 0.0)
    p_low = p.astype(jnp.bfloat16)
    att = jnp.dot(p_low, v, preferred_element_type=jnp.float32)
    gp = lax.dot_general(g, v, NT, preferred_element_type=jnp.float32)
    delta = jnp.sum(p * gp, axis=1, keepdims=True)
    gs = (p * (gp - delta) * scale).astype(jnp.bfloat16)
    gq = jnp.dot(gs, k, preferred_element_type=jnp.float32)
    dk = lax.dot_general(gs, q, TN, preferred_element_type=jnp.float32)
    dv = lax.dot_general(p_low, g, TN, preferred_element_type=jnp.float32)
    dkv = jnp.concatenate([dk, dv], axis=1)
    for t, u in enumerate(units):
        acc_ref[u] += dkv[SPAN * t:SPAN * (t + 1)]
    return att, gq


def _kernel(unroll, nb_ref, q_ref, g_ref, kv_ref, att_ref, gq_ref, grad_ref, acc_ref):
    pieces = q_ref.shape[0]
    acc_ref[...] = jnp.zeros(acc_ref.shape, acc_ref.dtype)
    scale = 1.0 / math.sqrt(HD)
    row = lax.broadcasted_iota(jnp.int32, (SPAN, 1), 0)
    first = row == 0
    last = row == SPAN - 1
    down = lambda x: pltpu.roll(x, 1, 0)
    up = lambda x: pltpu.roll(x, SPAN - 1, 0)
    lo = pl.ds(0, SPAN)
    hi = pl.ds(SPAN, SPAN)

    def tiles(ref, piece, prev):
        a = down(ref[piece, lo, :].astype(jnp.float32))
        b = down(ref[piece, hi, :].astype(jnp.float32))
        c = down(ref[prev, hi, :].astype(jnp.float32))
        even = jnp.where(first, a, b).astype(jnp.bfloat16)
        odd = jnp.where(first, c, a).astype(jnp.bfloat16)
        return even, odd

    def put(ref, piece, prev, even, odd):
        e = up(even)
        o = up(odd)
        ref[piece, lo, :] = jnp.where(last, e, o).astype(ref.dtype)
        kept = ref[piece, hi, :].astype(jnp.float32)
        ref[piece, hi, :] = jnp.where(last, kept, e).astype(ref.dtype)
        before = ref[prev, hi, :].astype(jnp.float32)
        ref[prev, hi, :] = jnp.where(last, o, before).astype(ref.dtype)

    def body(piece, carry):
        prev = (piece + pieces - 1) % pieces
        q_even, q_odd = tiles(q_ref, piece, prev)
        g_even, g_odd = tiles(g_ref, piece, prev)
        att_e, gq_e = _span(q_even, g_even, kv_ref, acc_ref, nb_ref, 2 * piece, None, scale)
        odd_span = (2 * piece + 2 * pieces - 1) % (2 * pieces)
        valid = first | (piece >= 1)
        att_o, gq_o = _span(q_odd, g_odd, kv_ref, acc_ref, nb_ref, odd_span, valid, scale)
        put(att_ref, piece, prev, att_e, att_o)
        put(gq_ref, piece, prev, gq_e, gq_o)
        return carry

    lax.fori_loop(0, pieces, body, 0, unroll=unroll)
    grad_ref[...] = acc_ref[...].astype(grad_ref.dtype)


def attend(nb, q, g, kv, unroll=8):
    pieces, rows, lanes = q.shape
    units = kv.shape[0]
    whole_q = pl.BlockSpec(q.shape, lambda j, nb: (0, 0, 0))
    whole_kv = pl.BlockSpec(kv.shape, lambda j, nb: (0, 0, 0))
    acc_shape = (units, SPAN, 2 * HD)
    whole_acc = pl.BlockSpec(acc_shape, lambda j, nb: (0, 0, 0))
    flops = pieces * rows * 4 * SPAN * HD * 2 * 6
    bytes_accessed = 4 * q.size * 2 + kv.size * 2 + math.prod(acc_shape) * 2
    call = pl.pallas_call(
        functools.partial(_kernel, unroll),
        grid_spec=pltpu.PrefetchScalarGridSpec(
            num_scalar_prefetch=1,
            grid=(1,),
            in_specs=[whole_q, whole_q, whole_kv],
            out_specs=[whole_q, whole_q, whole_acc],
            scratch_shapes=[pltpu.VMEM(acc_shape, jnp.float32)],
        ),
        out_shape=[
            jax.ShapeDtypeStruct(q.shape, jnp.bfloat16),
            jax.ShapeDtypeStruct(q.shape, jnp.bfloat16),
            jax.ShapeDtypeStruct(acc_shape, jnp.bfloat16),
        ],
        compiler_params=pltpu.CompilerParams(
            dimension_semantics=("arbitrary",), vmem_limit_bytes=56 * 1024 * 1024
        ),
        cost_estimate=pl.CostEstimate(
            flops=flops, transcendentals=pieces * rows * 4 * SPAN, bytes_accessed=bytes_accessed
        ),
        name="attend",
    )
    return call(nb, q, g, kv)


def local(queries, cotangent, states, neighbours):
    parts = lax.axis_size("seq")
    groups = lax.axis_size("dp")
    tok_dev = queries.shape[1]
    width = queries.shape[2]
    heads = width // HD
    quarter = SPAN // groups
    member = lax.axis_index("dp")

    st = states.reshape(SPAN, 2, heads, HD)
    st = lax.dynamic_slice_in_dim(st, member * quarter, quarter, axis=0)[None]
    moved = lax.all_to_all(st, "seq", split_axis=3, concat_axis=0, tiled=True)
    kv = lax.all_gather(moved, "dp", axis=1, tiled=True).reshape(parts, SPAN, 2 * HD)
    nb = neighbours.reshape(-1)

    def heads_in(x):
        x = lax.all_to_all(x.reshape(tok_dev, heads, HD), "seq", split_axis=1, concat_axis=0, tiled=True)
        return x.reshape(parts, tok_dev, HD)

    def heads_out(x):
        rows = x.shape[1]
        x = lax.all_to_all(x.reshape(parts, rows, 1, HD), "seq", split_axis=0, concat_axis=2, tiled=True)
        return x.reshape(rows, width)

    att, gq, acc = attend(nb, heads_in(queries), heads_in(cotangent), kv)
    red = lax.psum_scatter(acc, "dp", scatter_dimension=1, tiled=True)
    attended = heads_out(att).reshape(1, tok_dev, width)
    both = heads_out(jnp.concatenate([gq, red.reshape(parts, 2 * quarter, HD)], axis=1))
    query_grad = both[:tok_dev].reshape(1, tok_dev, width)
    home = both[tok_dev:].reshape(quarter, 2 * width)
    state_grad = lax.all_gather(home, "dp", axis=0, tiled=True).reshape(1, SPAN, 2 * width)
    return (attended, query_grad, state_grad)


def solution(mesh):
    placed = (P("dp", "seq", None), P("dp", "seq", None), P("seq", None, None), P("dp", None, None))
    return jax.shard_map(
        local,
        mesh=mesh,
        in_specs=placed,
        out_specs=(P("dp", "seq", None), P("dp", "seq", None), P("seq", None, None)),
        check_vma=False,
    )
```

```python
import functools
import math

import jax
import jax.numpy as jnp
from jax import lax
from jax.experimental import pallas as pl
from jax.experimental.pallas import tpu as pltpu
from jax.sharding import PartitionSpec as P

SPAN = 64
HD = 128
NT = (((1,), (1,)), ((), ()))
TN = (((0,), (0,)), ((), ()))


def _span(q, g, kv_ref, acc_ref, nb_ref, span, valid, scale):
    u0 = nb_ref[2 * span]
    u1 = nb_ref[2 * span + 1]
    units = (u0, u0 + 1, u1, u1 + 1)
    kv = jnp.concatenate([kv_ref[u] for u in units], axis=0)
    k = kv[:, :HD]
    v = kv[:, HD:]
    s = lax.dot_general(q, k, NT, preferred_element_type=jnp.float32) * scale
    top = jnp.max(s, axis=1, keepdims=True)
    e = jnp.exp(s - top)
    p = e / jnp.sum(e, axis=1, keepdims=True)
    if valid is not None:
        p = jnp.where(valid, p, 0.0)
    p_low = p.astype(jnp.bfloat16)
    att = jnp.dot(p_low, v, preferred_element_type=jnp.float32)
    gp = lax.dot_general(g, v, NT, preferred_element_type=jnp.float32)
    delta = jnp.sum(p * gp, axis=1, keepdims=True)
    gs = (p * (gp - delta) * scale).astype(jnp.bfloat16)
    gq = jnp.dot(gs, k, preferred_element_type=jnp.float32)
    dk = lax.dot_general(gs, q, TN, preferred_element_type=jnp.float32)
    dv = lax.dot_general(p_low, g, TN, preferred_element_type=jnp.float32)
    dkv = jnp.concatenate([dk, dv], axis=1)
    for t, u in enumerate(units):
        acc_ref[u] += dkv[SPAN * t:SPAN * (t + 1)]
    return att, gq


def _kernel(unroll, nb_ref, q_ref, g_ref, kv_ref, att_ref, gq_ref, grad_ref, acc_ref):
    pieces = q_ref.shape[0]
    acc_ref[...] = jnp.zeros(acc_ref.shape, acc_ref.dtype)
    scale = 1.0 / math.sqrt(HD)
    row = lax.broadcasted_iota(jnp.int32, (SPAN, 1), 0)
    first = row == 0
    last = row == SPAN - 1
    down = lambda x: pltpu.roll(x, 1, 0)
    up = lambda x: pltpu.roll(x, SPAN - 1, 0)
    lo = pl.ds(0, SPAN)
    hi = pl.ds(SPAN, SPAN)

    def tiles(ref, piece, prev):
        a = down(ref[piece, lo, :].astype(jnp.float32))
        b = down(ref[piece, hi, :].astype(jnp.float32))
        c = down(ref[prev, hi, :].astype(jnp.float32))
        even = jnp.where(first, a, b).astype(jnp.bfloat16)
        odd = jnp.where(first, c, a).astype(jnp.bfloat16)
        return even, odd

    def put(ref, piece, prev, even, odd):
        e = up(even)
        o = up(odd)
        ref[piece, lo, :] = jnp.where(last, e, o).astype(ref.dtype)
        kept = ref[piece, hi, :].astype(jnp.float32)
        ref[piece, hi, :] = jnp.where(last, kept, e).astype(ref.dtype)
        before = ref[prev, hi, :].astype(jnp.float32)
        ref[prev, hi, :] = jnp.where(last, o, before).astype(ref.dtype)

    def body(piece, carry):
        prev = (piece + pieces - 1) % pieces
        q_even, q_odd = tiles(q_ref, piece, prev)
        g_even, g_odd = tiles(g_ref, piece, prev)
        att_e, gq_e = _span(q_even, g_even, kv_ref, acc_ref, nb_ref, 2 * piece, None, scale)
        odd_span = (2 * piece + 2 * pieces - 1) % (2 * pieces)
        valid = first | (piece >= 1)
        att_o, gq_o = _span(q_odd, g_odd, kv_ref, acc_ref, nb_ref, odd_span, valid, scale)
        put(att_ref, piece, prev, att_e, att_o)
        put(gq_ref, piece, prev, gq_e, gq_o)
        return carry

    lax.fori_loop(0, pieces, body, 0, unroll=unroll)
    grad_ref[...] = acc_ref[...].astype(grad_ref.dtype)


def attend(nb, q, g, kv, unroll=8):
    pieces, _, lanes = q.shape
    rows = g.shape[1]
    units = kv.shape[0]
    whole_in = pl.BlockSpec(q.shape, lambda j, nb: (0, 0, 0))
    whole_q = pl.BlockSpec(g.shape, lambda j, nb: (0, 0, 0))
    whole_kv = pl.BlockSpec(kv.shape, lambda j, nb: (0, 0, 0))
    acc_shape = (units, SPAN, 2 * HD)
    whole_acc = pl.BlockSpec(acc_shape, lambda j, nb: (0, 0, 0))
    flops = pieces * rows * 4 * SPAN * HD * 2 * 6
    bytes_accessed = 4 * g.size * 2 + kv.size * 2 + math.prod(acc_shape) * 2
    call = pl.pallas_call(
        functools.partial(_kernel, unroll),
        grid_spec=pltpu.PrefetchScalarGridSpec(
            num_scalar_prefetch=1,
            grid=(1,),
            in_specs=[whole_in, whole_q, whole_kv],
            out_specs=[whole_q, whole_q, whole_acc],
            scratch_shapes=[pltpu.VMEM(acc_shape, jnp.float32)],
        ),
        out_shape=[
            jax.ShapeDtypeStruct(g.shape, jnp.bfloat16),
            jax.ShapeDtypeStruct(g.shape, jnp.bfloat16),
            jax.ShapeDtypeStruct(acc_shape, jnp.bfloat16),
        ],
        compiler_params=pltpu.CompilerParams(
            dimension_semantics=("arbitrary",), vmem_limit_bytes=56 * 1024 * 1024
        ),
        cost_estimate=pl.CostEstimate(
            flops=flops, transcendentals=pieces * rows * 4 * SPAN, bytes_accessed=bytes_accessed
        ),
        name="attend",
    )
    return call(nb, q, g, kv)


def local(queries, cotangent, states, neighbours):
    parts = lax.axis_size("seq")
    groups = lax.axis_size("dp")
    tok_dev = queries.shape[1]
    width = queries.shape[2]
    heads = width // HD
    quarter = SPAN // groups
    member = lax.axis_index("dp")

    st = states.reshape(SPAN, 2, heads, HD)
    st = lax.dynamic_slice_in_dim(st, member * quarter, quarter, axis=0)
    nb = neighbours.reshape(-1)

    def heads_in(x):
        rows = x.shape[0]
        x = lax.all_to_all(x, "seq", split_axis=1, concat_axis=0, tiled=True)
        return x.reshape(parts, rows, HD)

    def heads_out(x):
        x = lax.all_to_all(x.reshape(parts, tok_dev, 1, HD), "seq", split_axis=0, concat_axis=2, tiled=True)
        return x.reshape(1, tok_dev, width)

    packed = jnp.concatenate(
        [queries.reshape(tok_dev, heads, HD), st.reshape(2 * quarter, heads, HD)], axis=0
    )
    q_in = heads_in(packed)
    moved = q_in[:, tok_dev:].reshape(parts, quarter, 2, 1, HD)
    kv = lax.all_gather(moved, "dp", axis=1, tiled=True).reshape(parts, SPAN, 2 * HD)
    att, gq, acc = attend(nb, q_in, heads_in(cotangent.reshape(tok_dev, heads, HD)), kv)
    red = lax.psum_scatter(acc, "dp", scatter_dimension=1, tiled=True)
    attended = heads_out(att)
    query_grad = heads_out(gq)

    home = lax.all_to_all(red, "seq", split_axis=0, concat_axis=0, tiled=True)
    home = home.reshape(heads, quarter, 2, HD).transpose(1, 2, 0, 3).reshape(quarter, 2 * width)
    state_grad = lax.all_gather(home, "dp", axis=0, tiled=True).reshape(1, SPAN, 2 * width)
    return (attended, query_grad, state_grad)


def solution(mesh):
    placed = (P("dp", "seq", None), P("dp", "seq", None), P("seq", None, None), P("dp", None, None))
    return jax.shard_map(
        local,
        mesh=mesh,
        in_specs=placed,
        out_specs=(P("dp", "seq", None), P("dp", "seq", None), P("seq", None, None)),
        check_vma=False,
    )
```

```python
import functools
import math

import jax
import jax.numpy as jnp
from jax import lax
from jax.experimental import pallas as pl
from jax.experimental.pallas import tpu as pltpu
from jax.sharding import PartitionSpec as P

SPAN = 64
HD = 128
NT = (((1,), (1,)), ((), ()))
TN = (((0,), (0,)), ((), ()))


def _span(q, g, kv_ref, acc_ref, nb_ref, span, valid, scale):
    u0 = nb_ref[2 * span]
    u1 = nb_ref[2 * span + 1]
    units = (u0, u0 + 1, u1, u1 + 1)
    kv = jnp.concatenate([kv_ref[u] for u in units], axis=0)
    k = kv[:, :HD]
    v = kv[:, HD:]
    s = lax.dot_general(q, k, NT, preferred_element_type=jnp.float32) * scale
    top = jnp.max(s, axis=1, keepdims=True)
    e = jnp.exp(s - top)
    p = e / jnp.sum(e, axis=1, keepdims=True)
    if valid is not None:
        p = jnp.where(valid, p, 0.0)
    p_low = p.astype(jnp.bfloat16)
    att = jnp.dot(p_low, v, preferred_element_type=jnp.float32)
    gp = lax.dot_general(g, v, NT, preferred_element_type=jnp.float32)
    delta = jnp.sum(p * gp, axis=1, keepdims=True)
    gs = (p * (gp - delta) * scale).astype(jnp.bfloat16)
    gq = jnp.dot(gs, k, preferred_element_type=jnp.float32)
    dk = lax.dot_general(gs, q, TN, preferred_element_type=jnp.float32)
    dv = lax.dot_general(p_low, g, TN, preferred_element_type=jnp.float32)
    dkv = jnp.concatenate([dk, dv], axis=1)
    for t, u in enumerate(units):
        acc_ref[u] += dkv[SPAN * t:SPAN * (t + 1)]
    return att, gq


def _kernel(unroll, nb_ref, q_ref, g_ref, kv_ref, att_ref, gq_ref, grad_ref, acc_ref):
    pieces = q_ref.shape[0]
    acc_ref[...] = jnp.zeros(acc_ref.shape, acc_ref.dtype)
    scale = 1.0 / math.sqrt(HD)
    row = lax.broadcasted_iota(jnp.int32, (SPAN, 1), 0)
    first = row == 0
    last = row == SPAN - 1
    down = lambda x: pltpu.roll(x, 1, 0)
    up = lambda x: pltpu.roll(x, SPAN - 1, 0)
    lo = pl.ds(0, SPAN)
    hi = pl.ds(SPAN, SPAN)

    def tiles(ref, piece, prev):
        a = down(ref[piece, lo, :].astype(jnp.float32))
        b = down(ref[piece, hi, :].astype(jnp.float32))
        c = down(ref[prev, hi, :].astype(jnp.float32))
        even = jnp.where(first, a, b).astype(jnp.bfloat16)
        odd = jnp.where(first, c, a).astype(jnp.bfloat16)
        return even, odd

    def put(ref, piece, prev, even, odd):
        e = up(even)
        o = up(odd)
        ref[piece, lo, :] = jnp.where(last, e, o).astype(ref.dtype)
        kept = ref[piece, hi, :].astype(jnp.float32)
        ref[piece, hi, :] = jnp.where(last, kept, e).astype(ref.dtype)
        before = ref[prev, hi, :].astype(jnp.float32)
        ref[prev, hi, :] = jnp.where(last, o, before).astype(ref.dtype)

    def body(piece, carry):
        prev = (piece + pieces - 1) % pieces
        q_even, q_odd = tiles(q_ref, piece, prev)
        g_even, g_odd = tiles(g_ref, piece, prev)
        att_e, gq_e = _span(q_even, g_even, kv_ref, acc_ref, nb_ref, 2 * piece, None, scale)
        odd_span = (2 * piece + 2 * pieces - 1) % (2 * pieces)
        valid = first | (piece >= 1)
        att_o, gq_o = _span(q_odd, g_odd, kv_ref, acc_ref, nb_ref, odd_span, valid, scale)
        put(att_ref, piece, prev, att_e, att_o)
        put(gq_ref, piece, prev, gq_e, gq_o)
        return carry

    lax.fori_loop(0, pieces, body, 0, unroll=unroll)
    grad_ref[...] = acc_ref[...].astype(grad_ref.dtype)


def attend(nb, q, g, kv, unroll=16):
    pieces, _, lanes = q.shape
    rows = g.shape[1]
    units = kv.shape[0]
    whole_in = pl.BlockSpec(q.shape, lambda j, nb: (0, 0, 0))
    whole_q = pl.BlockSpec(g.shape, lambda j, nb: (0, 0, 0))
    whole_kv = pl.BlockSpec(kv.shape, lambda j, nb: (0, 0, 0))
    acc_shape = (units, SPAN, 2 * HD)
    whole_acc = pl.BlockSpec(acc_shape, lambda j, nb: (0, 0, 0))
    flops = pieces * rows * 4 * SPAN * HD * 2 * 6
    bytes_accessed = 4 * g.size * 2 + kv.size * 2 + math.prod(acc_shape) * 2
    call = pl.pallas_call(
        functools.partial(_kernel, unroll),
        grid_spec=pltpu.PrefetchScalarGridSpec(
            num_scalar_prefetch=1,
            grid=(1,),
            in_specs=[whole_in, whole_q, whole_kv],
            out_specs=[whole_q, whole_q, whole_acc],
            scratch_shapes=[pltpu.VMEM(acc_shape, jnp.float32)],
        ),
        out_shape=[
            jax.ShapeDtypeStruct(g.shape, jnp.bfloat16),
            jax.ShapeDtypeStruct(g.shape, jnp.bfloat16),
            jax.ShapeDtypeStruct(acc_shape, jnp.bfloat16),
        ],
        compiler_params=pltpu.CompilerParams(
            dimension_semantics=("arbitrary",), vmem_limit_bytes=56 * 1024 * 1024
        ),
        cost_estimate=pl.CostEstimate(
            flops=flops, transcendentals=pieces * rows * 4 * SPAN, bytes_accessed=bytes_accessed
        ),
        name="attend",
    )
    return call(nb, q, g, kv)


def local(queries, cotangent, states, neighbours):
    parts = lax.axis_size("seq")
    groups = lax.axis_size("dp")
    tok_dev = queries.shape[1]
    width = queries.shape[2]
    heads = width // HD
    quarter = SPAN // groups
    member = lax.axis_index("dp")

    st = states.reshape(SPAN, 2, heads, HD)
    st = lax.dynamic_slice_in_dim(st, member * quarter, quarter, axis=0)
    nb = neighbours.reshape(-1)

    def heads_in(x):
        rows = x.shape[0]
        x = lax.all_to_all(x, "seq", split_axis=1, concat_axis=0, tiled=True)
        return x.reshape(parts, rows, HD)

    def heads_out(x):
        x = lax.all_to_all(x.reshape(parts, tok_dev, 1, HD), "seq", split_axis=0, concat_axis=2, tiled=True)
        return x.reshape(1, tok_dev, width)

    packed = jnp.concatenate(
        [queries.reshape(tok_dev, heads, HD), st.reshape(2 * quarter, heads, HD)], axis=0
    )
    q_in = heads_in(packed)
    moved = q_in[:, tok_dev:].reshape(parts, quarter, 2, 1, HD)
    kv = lax.all_gather(moved, "dp", axis=1, tiled=True).reshape(parts, SPAN, 2 * HD)
    att, gq, acc = attend(nb, q_in, heads_in(cotangent.reshape(tok_dev, heads, HD)), kv)
    red = lax.psum_scatter(acc, "dp", scatter_dimension=1, tiled=True)
    attended = heads_out(att)
    query_grad = heads_out(gq)

    home = lax.all_to_all(red, "seq", split_axis=0, concat_axis=0, tiled=True)
    home = home.reshape(heads, quarter, 2, HD).transpose(1, 2, 0, 3).reshape(quarter, 2 * width)
    state_grad = lax.all_gather(home, "dp", axis=0, tiled=True).reshape(1, SPAN, 2 * width)
    return (attended, query_grad, state_grad)


def solution(mesh):
    placed = (P("dp", "seq", None), P("dp", "seq", None), P("seq", None, None), P("dp", None, None))
    return jax.shard_map(
        local,
        mesh=mesh,
        in_specs=placed,
        out_specs=(P("dp", "seq", None), P("dp", "seq", None), P("seq", None, None)),
        check_vma=False,
    )
```
